512 devices in a mesh: dp: 32 (over z, core), seq: 16 (over x, y).
Axes of the slice: x: 4, y: 4, z: 16, core: 2. Of those that a mesh axis runs over, the one named last changes fastest.
Arguments:
- queries: bfloat16 [65536, 4096], P(('dp', 'seq')), may hold values from -9 to 9
- keys: bfloat16 [65536, 512], P(('dp', 'seq')), may hold values from -9 to 9
- values: bfloat16 [65536, 512], P(('dp', 'seq')), may hold values from -6 to 6
- grad_out: bfloat16 [65536, 4096], P(('dp', 'seq')), may hold values from -6 to 6
- doc_lengths: int32 [32, 32], replicated, may hold values from 1 to 128, 2048 in all within a row
- swap_mask: int32 [1], replicated, may hold values from 1 to 31
Outputs:
- grad_query: bfloat16 [65536, 4096], P(('dp', 'seq'))
- grad_key: bfloat16 [65536, 512], P(('dp', 'seq'))
- grad_value: bfloat16 [65536, 512], P(('dp', 'seq'))
The draws below stay inside these ranges and needn't reach their ends.
Inputs may be any that keep to these rules, and one draw needn't show every extreme that they name: `doc_lengths`: row p holds the lengths of the 32 documents of pack p in order; they sum to 2048 and the longest is 128. `swap_mask`: never zero.
All inputs are finite; a program needn't handle non-finite values.
Results may differ from the reference program's by a relative error of at most 0.0071.
Values may be sent and summed in bfloat16 or wider, within the bound.
No kernel may reach another device: no remote copies, remote signals or barrier semaphores. Data moves between devices by JAX's collectives and lax.ppermute only.
A program may use at most 64 MiB of HBM per device.

```python
import math
import jax
import jax.numpy as jnp
import numpy as np
from jax import lax

HQ = 32
KV = 4
DH = 128
PACK = 2048
DOCS = 32
MOST = 128
TOKENS = 65536
N_DP = 32


def shared_draw(key):
    base = jax.random.fold_in(key, 7)
    query_key, keys_key = jax.random.split(base, 2)
    queries = jnp.clip(jax.random.normal(query_key, (TOKENS, HQ * DH), jnp.float32), -6.0, 6.0)
    keys = jnp.clip(jax.random.normal(keys_key, (TOKENS, KV * DH), jnp.float32), -6.0, 6.0)
    return (queries, keys)


def draw_queries(key, part):
    return shared_draw(key)[0].astype(jnp.bfloat16)


def draw_keys(key, part):
    return shared_draw(key)[1].astype(jnp.bfloat16)


def steps_of(rng, dims, cuts, low, largest):
    factor_of = 1.0
    for dim, parts in cuts:
        steps = jax.random.uniform(jax.random.fold_in(jax.random.fold_in(rng, 6), dim), (parts,), jnp.float32, low / len(cuts), largest / len(cuts))
        factor_of = factor_of * jnp.repeat(jnp.exp(steps), dims[dim] // parts).reshape((-1,) + (1,) * (len(dims) - 1 - dim))
    return factor_of


def length_profile(amount, total, bound, lean):
    portions = [(1 << 20) // math.isqrt(grade ** lean) + 1 for grade in range(2, amount + 1)]
    surplus, holding = total - bound - (amount - 1), [1] * (amount - 1)
    while surplus > 0:
        movable = [i for i in range(amount - 1) if holding[i] < bound]
        mass, remaining = sum([portions[i] for i in movable]), surplus
        for i in movable:
            more = min(bound - holding[i], max(1, remaining * portions[i] // mass), surplus)
            holding[i] = holding[i] + more
            surplus = surplus - more
    return np.array([bound] + holding)


def uneven_parts(stream_key, count, total, most, lean):
    if count == 2:
        one = jax.random.randint(stream_key, (), max(1, total - most), min(most, total - 1) + 1)
        return jnp.stack([one, total - one])
    sizes = jnp.asarray(length_profile(count, total, most, lean), jnp.int32)
    twos = (count - 1) // 2
    source_of, taker = sizes[1:1 + 2 * twos:2], sizes[2:2 + 2 * twos:2]
    room = jnp.minimum(source_of - 1, most - taker)
    shifted = jax.random.randint(jax.random.fold_in(stream_key, 1), (twos,), 0, 1 << 20) % (room + 1)
    sizes = sizes.at[1:1 + 2 * twos:2].set(source_of - shifted).at[2:2 + 2 * twos:2].set(taker + shifted)
    return sizes[jax.random.permutation(jax.random.fold_in(stream_key, 2), count)]


def normal_values(stream_key, shape, deviation, most, cuts=(), held_as=jnp.bfloat16):
    gain = steps_of(stream_key, shape, cuts, -0.22, 0.18) if cuts else 1.0
    values = jax.random.normal(stream_key, shape, jnp.float32) * deviation * gain
    return jnp.minimum(jnp.maximum(values, -most), most).astype(held_as)


def setup_inputs(seed: int = 0) -> dict:
    key_of = jax.random.split(jax.random.key(seed), 7)
    return {
        "queries": draw_queries(jax.random.fold_in(key_of[6], 71), 0),
        "keys": draw_keys(jax.random.fold_in(key_of[6], 71), 0),
        "values": normal_values(key_of[2], (TOKENS, KV * DH), 1.0, 6.0, ((0, 512),)),
        "grad_out": normal_values(key_of[3], (TOKENS, HQ * DH), 1.0, 6.0, ((0, 512),)),
        "doc_lengths": jax.vmap(lambda own: uneven_parts(own, DOCS, PACK, MOST, 2))(jax.random.split(key_of[4], N_DP)).reshape((N_DP, DOCS)).astype(jnp.int32),
        "swap_mask": jax.random.randint(key_of[5], (1,), 1, N_DP).astype(jnp.int32),
    }


def group_grads(operands, allowed):
    query_group, key_group, value_group, grad_group = operands
    query_wide = query_group.astype(jnp.float32)
    key_wide = key_group.astype(jnp.float32)
    value_wide = value_group.astype(jnp.float32)
    grad_wide = grad_group.astype(jnp.float32)
    scale = DH ** -0.5
    scores = jnp.einsum("igd,jd->gij", query_wide, key_wide) * scale
    scores = jnp.where(allowed[None], scores, -1e30)
    peak = jnp.max(scores, axis=2, keepdims=True)
    expo = jnp.where(allowed[None], jnp.exp(scores - peak), 0.0)
    probs = expo / jnp.sum(expo, axis=2, keepdims=True)
    probs_low = lax.optimization_barrier(probs.astype(jnp.bfloat16)).astype(jnp.float32)
    dprobs = jnp.einsum("igd,jd->gij", grad_wide, value_wide)
    delta = jnp.sum(probs * dprobs, axis=2, keepdims=True)
    dscores = lax.optimization_barrier((probs * (dprobs - delta)).astype(jnp.bfloat16)).astype(jnp.float32)
    pack_dq = (jnp.einsum("gij,jd->igd", dscores, key_wide) * scale).astype(jnp.bfloat16)
    pack_dk = (jnp.einsum("gij,igd->jd", dscores, query_wide) * scale).astype(jnp.bfloat16)
    pack_dv = jnp.einsum("gij,igd->jd", probs_low, grad_wide).astype(jnp.bfloat16)
    return pack_dq, pack_dk, pack_dv


def pack_grads(operands):
    query_pack, key_pack, value_pack, grad_pack, lengths = operands
    ends = jnp.cumsum(lengths)
    positions = jnp.arange(PACK, dtype=jnp.int32)
    segment = jnp.sum((ends[None, :] <= positions[:, None]).astype(jnp.int32), axis=1)
    allowed = (positions[None, :] <= positions[:, None]) & (segment[None, :] == segment[:, None])
    grouped = (jnp.moveaxis(query_pack, 1, 0), jnp.moveaxis(key_pack, 1, 0), jnp.moveaxis(value_pack, 1, 0), jnp.moveaxis(grad_pack, 1, 0))
    pack_dq, pack_dk, pack_dv = lax.map(lambda group_ops: group_grads(group_ops, allowed), grouped)
    return jnp.moveaxis(pack_dq, 0, 1), jnp.moveaxis(pack_dk, 0, 1), jnp.moveaxis(pack_dv, 0, 1)


def reference(queries, keys, values, grad_out, doc_lengths, swap_mask):
    group = HQ // KV
    query_all = queries.reshape(N_DP, PACK, KV, group, DH)
    grad_all = grad_out.reshape(N_DP, PACK, KV, group, DH)
    key_all = keys.reshape(N_DP, PACK, KV, DH)
    value_all = values.reshape(N_DP, PACK, KV, DH)
    dq_all, dk_all, dv_all = lax.map(pack_grads, (query_all, key_all, value_all, grad_all, doc_lengths))
    order = jnp.bitwise_xor(jnp.arange(N_DP, dtype=jnp.int32), swap_mask[0].astype(jnp.int32))
    grad_query = dq_all[order].reshape(N_DP * PACK, HQ * DH)
    grad_key = dk_all[order].reshape(N_DP * PACK, KV * DH)
    grad_value = dv_all[order].reshape(N_DP * PACK, KV * DH)
    return grad_query, grad_key, grad_value
```

```python
import jax
import jax.numpy as jnp
from jax import lax
from jax.sharding import PartitionSpec as P

HQ = 32
KV = 4
DH = 128


def product(left, right, spec):
    return jnp.einsum(spec, left, right, preferred_element_type=jnp.float32)


def paired(block, axis, mask):
    count = lax.axis_size(axis)

    def route(m):
        return lambda x: lax.ppermute(x, axis, [(d, d ^ m) for d in range(count)])

    branches = [route(m) for m in range(1, count)]
    return lax.switch(mask - 1, branches, block)


def body(queries, keys, values, grad_out, doc_lengths, swap_mask):
    seq_count = lax.axis_size("seq")
    rows = queries.shape[0]
    group = HQ // KV
    scale = DH ** (-0.5)
    s = lax.axis_index("seq")
    dp = lax.axis_index("dp")

    kv_own = jnp.concatenate([keys, values], axis=1)
    kv_prev = lax.ppermute(kv_own, "seq", [(i, i + 1) for i in range(seq_count - 1)])
    key_band = jnp.concatenate([kv_prev[:, : KV * DH], keys], axis=0).reshape(2 * rows, KV, DH)
    value_band = jnp.concatenate([kv_prev[:, KV * DH :], values], axis=0).reshape(2 * rows, KV, DH)

    lengths = lax.dynamic_slice_in_dim(doc_lengths, dp, 1, 0)[0]
    ends = jnp.cumsum(lengths)
    q_pos = s * rows + jnp.arange(rows, dtype=jnp.int32)
    k_pos = s * rows - rows + jnp.arange(2 * rows, dtype=jnp.int32)
    seg_q = jnp.sum((ends[None, :] <= q_pos[:, None]).astype(jnp.int32), axis=1)
    seg_k = jnp.sum((ends[None, :] <= k_pos[:, None]).astype(jnp.int32), axis=1)
    allowed = (
        (k_pos[None, :] <= q_pos[:, None])
        & (k_pos[None, :] >= 0)
        & (seg_k[None, :] == seg_q[:, None])
    )
    allowed = allowed[None, :, None, :]

    q = queries.reshape(rows, KV, group, DH)
    do = grad_out.reshape(rows, KV, group, DH)
    scores = product(q, key_band, "tghd,sgd->gths")
    dprobs = product(do, value_band, "tghd,sgd->gths")
    scores = jnp.where(allowed, scores * scale, -1e30)
    peak = jnp.max(scores, axis=3, keepdims=True)
    expo = jnp.where(allowed, jnp.exp(scores - peak), 0.0)
    probs = expo / jnp.sum(expo, axis=3, keepdims=True)
    probs_low = probs.astype(jnp.bfloat16)
    delta = jnp.sum(probs * dprobs, axis=3, keepdims=True)
    dscores = (probs * (dprobs - delta)).astype(jnp.bfloat16)

    dq = (product(dscores, key_band, "gths,sgd->tghd") * scale).astype(jnp.bfloat16)
    dk_band = product(dscores, q, "gths,tghd->sgd") * scale
    dv_band = product(probs_low, do, "gths,tghd->sgd")

    back = jnp.concatenate(
        [dk_band[:rows].reshape(rows, KV * DH), dv_band[:rows].reshape(rows, KV * DH)], axis=1
    )
    back = lax.ppermute(back, "seq", [(i + 1, i) for i in range(seq_count - 1)])
    dk = (dk_band[rows:].reshape(rows, KV * DH) + back[:, : KV * DH]).astype(jnp.bfloat16)
    dv = (dv_band[rows:].reshape(rows, KV * DH) + back[:, KV * DH :]).astype(jnp.bfloat16)

    out = jnp.concatenate([dq.reshape(rows, HQ * DH), dk, dv], axis=1)
    out = paired(out, "dp", swap_mask[0])
    return out[:, : HQ * DH], out[:, HQ * DH : HQ * DH + KV * DH], out[:, HQ * DH + KV * DH :]


def solution(mesh):
    return jax.shard_map(
        body,
        mesh=mesh,
        in_specs=(
            P(("dp", "seq"), None),
            P(("dp", "seq"), None),
            P(("dp", "seq"), None),
            P(("dp", "seq"), None),
            P(),
            P(),
        ),
        out_specs=(P(("dp", "seq"), None), P(("dp", "seq"), None), P(("dp", "seq"), None)),
        check_vma=False,
    )
```

```python
import functools

import jax
import jax.numpy as jnp
from jax import lax
from jax.experimental import pallas as pl
from jax.experimental.pallas import tpu as pltpu
from jax.sharding import PartitionSpec as P

HQ = 32
KV = 4
DH = 128
INTERPRET = False

contract_last = (((1,), (1,)), ((), ()))
contract_inner = (((1,), (0,)), ((), ()))
contract_first = (((0,), (0,)), ((), ()))


def product(left, right, dims):
    return lax.dot_general(left, right, dims, preferred_element_type=jnp.float32)


def group_kernel(q_ref, do_ref, k_ref, v_ref, mask_ref, dq_ref, dk_ref, dv_ref):
    scale = DH ** (-0.5)
    group = HQ // KV
    key_band = k_ref[...]
    value_band = v_ref[...]
    allowed = mask_ref[...] != 0
    dk_acc = jnp.zeros(dk_ref.shape, jnp.float32)
    dv_acc = jnp.zeros(dv_ref.shape, jnp.float32)
    for h in range(group):
        cols = slice(h * DH, (h + 1) * DH)
        q = q_ref[:, cols]
        do = do_ref[:, cols]
        scores = product(q, key_band, contract_last)
        dprobs = product(do, value_band, contract_last)
        scores = jnp.where(allowed, scores * scale, -1e30)
        peak = jnp.max(scores, axis=1, keepdims=True)
        expo = jnp.where(allowed, jnp.exp(scores - peak), 0.0)
        probs = expo / jnp.sum(expo, axis=1, keepdims=True)
        delta = jnp.sum(probs * dprobs, axis=1, keepdims=True)
        dscores = (probs * (dprobs - delta)).astype(jnp.bfloat16)
        dq_ref[:, cols] = (product(dscores, key_band, contract_inner) * scale).astype(jnp.bfloat16)
        dk_acc = dk_acc + product(dscores, q, contract_first)
        dv_acc = dv_acc + product(probs.astype(jnp.bfloat16), do, contract_first)
    dk_ref[...] = dk_acc * scale
    dv_ref[...] = dv_acc


def attention_grads(queries, grad_out, key_band, value_band, mask):
    rows = queries.shape[0]
    band = key_band.shape[0]
    width = (HQ // KV) * DH
    wide = pl.BlockSpec((rows, width), lambda g: (0, g))
    narrow = pl.BlockSpec((band, DH), lambda g: (0, g))
    return pl.pallas_call(
        group_kernel,
        grid=(KV,),
        in_specs=[wide, wide, narrow, narrow, pl.BlockSpec((rows, band), lambda g: (0, 0))],
        out_specs=[wide, narrow, narrow],
        out_shape=[
            jax.ShapeDtypeStruct((rows, HQ * DH), jnp.bfloat16),
            jax.ShapeDtypeStruct((band, KV * DH), jnp.float32),
            jax.ShapeDtypeStruct((band, KV * DH), jnp.float32),
        ],
        interpret=INTERPRET,
    )(queries, grad_out, key_band, value_band, mask)


def paired(blocks, axis, mask):
    count = lax.axis_size(axis)

    def route(m):
        pairs = [(d, d ^ m) for d in range(count)]
        return lambda xs: tuple(lax.ppermute(x, axis, pairs) for x in xs)

    return lax.switch(mask - 1, [route(m) for m in range(1, count)], blocks)


def body(queries, keys, values, grad_out, doc_lengths, swap_mask):
    seq_count = lax.axis_size("seq")
    rows = queries.shape[0]
    s = lax.axis_index("seq")
    dp = lax.axis_index("dp")

    kv_own = jnp.concatenate([keys, values], axis=1)
    kv_prev = lax.ppermute(kv_own, "seq", [(i, i + 1) for i in range(seq_count - 1)])
    key_band = jnp.concatenate([kv_prev[:, : KV * DH], keys], axis=0)
    value_band = jnp.concatenate([kv_prev[:, KV * DH :], values], axis=0)

    lengths = lax.dynamic_slice_in_dim(doc_lengths, dp, 1, 0)[0]
    ends = jnp.cumsum(lengths)
    q_pos = s * rows + jnp.arange(rows, dtype=jnp.int32)
    k_pos = s * rows - rows + jnp.arange(2 * rows, dtype=jnp.int32)
    seg_q = jnp.sum((ends[None, :] <= q_pos[:, None]).astype(jnp.int32), axis=1)
    seg_k = jnp.sum((ends[None, :] <= k_pos[:, None]).astype(jnp.int32), axis=1)
    allowed = (
        (k_pos[None, :] <= q_pos[:, None])
        & (k_pos[None, :] >= 0)
        & (seg_k[None, :] == seg_q[:, None])
    )

    dq, dk_band, dv_band = attention_grads(queries, grad_out, key_band, value_band, allowed.astype(jnp.int32))

    back = jnp.concatenate([dk_band[:rows], dv_band[:rows]], axis=1)
    back = lax.ppermute(back, "seq", [(i + 1, i) for i in range(seq_count - 1)])
    dk = (dk_band[rows:] + back[:, : KV * DH]).astype(jnp.bfloat16)
    dv = (dv_band[rows:] + back[:, KV * DH :]).astype(jnp.bfloat16)
    return paired((dq, dk, dv), "dp", swap_mask[0])


def solution(mesh):
    return jax.shard_map(
        body,
        mesh=mesh,
        in_specs=(
            P(("dp", "seq"), None),
            P(("dp", "seq"), None),
            P(("dp", "seq"), None),
            P(("dp", "seq"), None),
            P(),
            P(),
        ),
        out_specs=(P(("dp", "seq"), None), P(("dp", "seq"), None), P(("dp", "seq"), None)),
        check_vma=False,
    )
```

```python
import jax
import jax.numpy as jnp
from jax import lax
from jax.experimental import pallas as pl
from jax.experimental.pallas import tpu as pltpu
from jax.sharding import PartitionSpec as P

HQ = 32
KV = 4
DH = 128
INTERPRET = False

contract_last = (((1,), (1,)), ((), ()))
contract_inner = (((1,), (0,)), ((), ()))
contract_first = (((0,), (0,)), ((), ()))


def product(left, right, dims):
    return lax.dot_general(left, right, dims, preferred_element_type=jnp.float32)


def group_kernel(q_ref, do_ref, k_ref, v_ref, mask_ref, dq_ref, dk_ref, dv_ref):
    scale = DH ** (-0.5)
    group = HQ // KV
    key_band = k_ref[...]
    value_band = v_ref[...]
    allowed = mask_ref[...] != 0
    dk_acc = jnp.zeros(dk_ref.shape, jnp.float32)
    dv_acc = jnp.zeros(dv_ref.shape, jnp.float32)
    for h in range(group):
        cols = slice(h * DH, (h + 1) * DH)
        q = q_ref[:, cols]
        do = do_ref[:, cols]
        scores = product(q, key_band, contract_last)
        dprobs = product(do, value_band, contract_last)
        scores = jnp.where(allowed, scores * scale, -1e30)
        peak = jnp.max(scores, axis=1, keepdims=True)
        expo = jnp.where(allowed, jnp.exp(scores - peak), 0.0)
        probs = expo * (1.0 / jnp.sum(expo, axis=1, keepdims=True))
        delta = jnp.sum(probs * dprobs, axis=1, keepdims=True)
        dscores = (probs * (dprobs - delta)).astype(jnp.bfloat16)
        dq_ref[:, cols] = (product(dscores, key_band, contract_inner) * scale).astype(jnp.bfloat16)
        dk_acc = dk_acc + product(dscores, q, contract_first)
        dv_acc = dv_acc + product(probs.astype(jnp.bfloat16), do, contract_first)
    dk_ref[...] = dk_acc * scale
    dv_ref[...] = dv_acc


def attention_grads(queries, grad_out, key_band, value_band, mask):
    rows = queries.shape[0]
    band = key_band.shape[0]
    width = (HQ // KV) * DH
    wide = pl.BlockSpec((rows, width), lambda g: (0, g))
    narrow = pl.BlockSpec((band, DH), lambda g: (0, g))
    return pl.pallas_call(
        group_kernel,
        grid=(KV,),
        in_specs=[wide, wide, narrow, narrow, pl.BlockSpec((rows, band), lambda g: (0, 0))],
        out_specs=[wide, narrow, narrow],
        out_shape=[
            jax.ShapeDtypeStruct((rows, HQ * DH), jnp.bfloat16),
            jax.ShapeDtypeStruct((band, KV * DH), jnp.float32),
            jax.ShapeDtypeStruct((band, KV * DH), jnp.float32),
        ],
        interpret=INTERPRET,
    )(queries, grad_out, key_band, value_band, mask)


def paired(dq, dk_band, dv_band, mask):
    dp_count = lax.axis_size("dp")
    seq_count = lax.axis_size("seq")
    rows = dq.shape[0]

    def route(m):
        pairs = [(d, d ^ m) for d in range(dp_count)]

        def run(ops):
            dq, dk_band, dv_band = ops
            dq = lax.ppermute(dq, "dp", pairs)
            back = jnp.concatenate([dk_band[:rows], dv_band[:rows]], axis=1)
            back = lax.ppermute(back, "seq", [(i + 1, i) for i in range(seq_count - 1)])
            own = jnp.concatenate([dk_band[rows:], dv_band[rows:]], axis=1)
            dkv = lax.ppermute((own + back).astype(jnp.bfloat16), "dp", pairs)
            return dq, dkv[:, : KV * DH], dkv[:, KV * DH :]

        return run

    return lax.switch(mask - 1, [route(m) for m in range(1, dp_count)], (dq, dk_band, dv_band))


def body(queries, keys, values, grad_out, doc_lengths, swap_mask):
    seq_count = lax.axis_size("seq")
    rows = queries.shape[0]
    s = lax.axis_index("seq")
    dp = lax.axis_index("dp")

    kv_own = jnp.concatenate([keys, values], axis=1)
    kv_prev = lax.ppermute(kv_own, "seq", [(i, i + 1) for i in range(seq_count - 1)])
    key_band = jnp.concatenate([kv_prev[:, : KV * DH], keys], axis=0)
    value_band = jnp.concatenate([kv_prev[:, KV * DH :], values], axis=0)

    lengths = lax.dynamic_slice_in_dim(doc_lengths, dp, 1, 0)[0]
    ends = jnp.cumsum(lengths)
    q_pos = s * rows + jnp.arange(rows, dtype=jnp.int32)
    k_pos = s * rows - rows + jnp.arange(2 * rows, dtype=jnp.int32)
    seg_q = jnp.sum((ends[None, :] <= q_pos[:, None]).astype(jnp.int32), axis=1)
    seg_k = jnp.sum((ends[None, :] <= k_pos[:, None]).astype(jnp.int32), axis=1)
    allowed = (
        (k_pos[None, :] <= q_pos[:, None])
        & (k_pos[None, :] >= 0)
        & (seg_k[None, :] == seg_q[:, None])
    )

    dq, dk_band, dv_band = attention_grads(queries, grad_out, key_band, value_band, allowed.astype(jnp.int32))
    return paired(dq, dk_band, dv_band, swap_mask[0])


def solution(mesh):
    return jax.shard_map(
        body,
        mesh=mesh,
        in_specs=(
            P(("dp", "seq"), None),
            P(("dp", "seq"), None),
            P(("dp", "seq"), None),
            P(("dp", "seq"), None),
            P(),
            P(),
        ),
        out_specs=(P(("dp", "seq"), None), P(("dp", "seq"), None), P(("dp", "seq"), None)),
        check_vma=False,
    )
```

```python
import jax
import jax.numpy as jnp
from jax import lax
from jax.experimental import pallas as pl
from jax.experimental.pallas import tpu as pltpu
from jax.sharding import PartitionSpec as P

HQ = 32
KV = 4
DH = 128
INTERPRET = False

contract_last = (((1,), (1,)), ((), ()))
contract_inner = (((1,), (0,)), ((), ()))
contract_first = (((0,), (0,)), ((), ()))


def product(left, right, dims):
    return lax.dot_general(left, right, dims, preferred_element_type=jnp.float32)


def group_kernel(q_ref, do_ref, k_ref, v_ref, mask_ref, dq_ref, dk_ref, dv_ref):
    scale = DH ** (-0.5)
    group = HQ // KV
    key_band = k_ref[...]
    value_band = v_ref[...]
    allowed = mask_ref[...] != 0
    dk_acc = jnp.zeros(dk_ref.shape, jnp.float32)
    dv_acc = jnp.zeros(dv_ref.shape, jnp.float32)
    for h in range(group):
        cols = slice(h * DH, (h + 1) * DH)
        q = q_ref[:, cols]
        do = do_ref[:, cols]
        scores = product(key_band, q, contract_last)
        dprobs = product(value_band, do, contract_last)
        scores = jnp.where(allowed, scores * scale, -1e30)
        peak = jnp.max(scores, axis=0, keepdims=True)
        expo = jnp.exp(scores - peak)
        probs = expo * (1.0 / jnp.sum(expo, axis=0, keepdims=True))
        delta = jnp.sum(probs * dprobs, axis=0, keepdims=True)
        dscores = (probs * (dprobs - delta)).astype(jnp.bfloat16)
        dq_ref[:, cols] = (product(dscores, key_band, contract_first) * scale).astype(jnp.bfloat16)
        dk_acc = dk_acc + product(dscores, q, contract_inner)
        dv_acc = dv_acc + product(probs.astype(jnp.bfloat16), do, contract_inner)
    dk_ref[...] = dk_acc * scale
    dv_ref[...] = dv_acc


def attention_grads(queries, grad_out, key_band, value_band, mask):
    rows = queries.shape[0]
    band = key_band.shape[0]
    width = (HQ // KV) * DH
    wide = pl.BlockSpec((rows, width), lambda g: (0, g))
    narrow = pl.BlockSpec((band, DH), lambda g: (0, g))
    return pl.pallas_call(
        group_kernel,
        grid=(KV,),
        in_specs=[wide, wide, narrow, narrow, pl.BlockSpec((band, rows), lambda g: (0, 0))],
        out_specs=[wide, narrow, narrow],
        out_shape=[
            jax.ShapeDtypeStruct((rows, HQ * DH), jnp.bfloat16),
            jax.ShapeDtypeStruct((band, KV * DH), jnp.float32),
            jax.ShapeDtypeStruct((band, KV * DH), jnp.float32),
        ],
        interpret=INTERPRET,
    )(queries, grad_out, key_band, value_band, mask)


def paired(dq, dk_band, dv_band, mask):
    dp_count = lax.axis_size("dp")
    seq_count = lax.axis_size("seq")
    rows = dq.shape[0]

    def route(m):
        pairs = [(d, d ^ m) for d in range(dp_count)]

        def run(ops):
            dq, dk_band, dv_band = ops
            dq = lax.ppermute(dq, "dp", pairs)
            back = jnp.concatenate([dk_band[:rows], dv_band[:rows]], axis=1)
            back = lax.ppermute(back, "seq", [(i + 1, i) for i in range(seq_count - 1)])
            own = jnp.concatenate([dk_band[rows:], dv_band[rows:]], axis=1)
            dkv = lax.ppermute((own + back).astype(jnp.bfloat16), "dp", pairs)
            return dq, dkv[:, : KV * DH], dkv[:, KV * DH :]

        return run

    return lax.switch(mask - 1, [route(m) for m in range(1, dp_count)], (dq, dk_band, dv_band))


def body(queries, keys, values, grad_out, doc_lengths, swap_mask):
    seq_count = lax.axis_size("seq")
    rows = queries.shape[0]
    s = lax.axis_index("seq")
    dp = lax.axis_index("dp")

    kv_own = jnp.concatenate([keys, values], axis=1)
    kv_prev = lax.ppermute(kv_own, "seq", [(i, i + 1) for i in range(seq_count - 1)])
    key_band = jnp.concatenate([kv_prev[:, : KV * DH], keys], axis=0)
    value_band = jnp.concatenate([kv_prev[:, KV * DH :], values], axis=0)

    lengths = lax.dynamic_slice_in_dim(doc_lengths, dp, 1, 0)[0]
    ends = jnp.cumsum(lengths)
    q_pos = s * rows + jnp.arange(rows, dtype=jnp.int32)
    k_pos = s * rows - rows + jnp.arange(2 * rows, dtype=jnp.int32)
    seg_q = jnp.sum((ends[None, :] <= q_pos[:, None]).astype(jnp.int32), axis=1)
    seg_k = jnp.sum((ends[None, :] <= k_pos[:, None]).astype(jnp.int32), axis=1)
    allowed = (
        (k_pos[None, :] <= q_pos[:, None])
        & (k_pos[None, :] >= 0)
        & (seg_k[None, :] == seg_q[:, None])
    )

    dq, dk_band, dv_band = attention_grads(queries, grad_out, key_band, value_band, allowed.T.astype(jnp.int32))
    return paired(dq, dk_band, dv_band, swap_mask[0])


def solution(mesh):
    return jax.shard_map(
        body,
        mesh=mesh,
        in_specs=(
            P(("dp", "seq"), None),
            P(("dp", "seq"), None),
            P(("dp", "seq"), None),
            P(("dp", "seq"), None),
            P(),
            P(),
        ),
        out_specs=(P(("dp", "seq"), None), P(("dp", "seq"), None), P(("dp", "seq"), None)),
        check_vma=False,
    )
```

```python
import jax
import jax.numpy as jnp
from jax import lax
from jax.experimental import pallas as pl
from jax.experimental.pallas import tpu as pltpu
from jax.sharding import PartitionSpec as P

HQ = 32
KV = 4
DH = 128
INTERPRET = False

contract_last = (((1,), (1,)), ((), ()))
contract_inner = (((1,), (0,)), ((), ()))
contract_first = (((0,), (0,)), ((), ()))


def product(left, right, dims):
    return lax.dot_general(left, right, dims, preferred_element_type=jnp.float32)


def group_kernel(q_ref, do_ref, kp_ref, vp_ref, k_ref, v_ref, mask_ref, dq_ref, dk_ref, dv_ref):
    scale = DH ** (-0.5)
    group = HQ // KV
    key_band = jnp.concatenate([kp_ref[...], k_ref[...]], axis=0)
    value_band = jnp.concatenate([vp_ref[...], v_ref[...]], axis=0)
    allowed = mask_ref[...] != 0
    dk_acc = jnp.zeros(dk_ref.shape, jnp.float32)
    dv_acc = jnp.zeros(dv_ref.shape, jnp.float32)
    for h in range(group):
        cols = slice(h * DH, (h + 1) * DH)
        q = q_ref[:, cols]
        do = do_ref[:, cols]
        scores = product(key_band, q, contract_last)
        dprobs = product(value_band, do, contract_last)
        scores = jnp.where(allowed, scores * scale, -1e30)
        peak = jnp.max(scores, axis=0, keepdims=True)
        expo = jnp.exp(scores - peak)
        probs = expo * (1.0 / jnp.sum(expo, axis=0, keepdims=True))
        delta = jnp.sum(probs * dprobs, axis=0, keepdims=True)
        dscores = (probs * (dprobs - delta)).astype(jnp.bfloat16)
        dq_ref[:, cols] = (product(dscores, key_band, contract_first) * scale).astype(jnp.bfloat16)
        dk_acc = dk_acc + product(dscores, q, contract_inner)
        dv_acc = dv_acc + product(probs.astype(jnp.bfloat16), do, contract_inner)
    dk_ref[...] = dk_acc * scale
    dv_ref[...] = dv_acc


def attention_grads(queries, grad_out, kv_prev, keys, values, mask):
    rows = queries.shape[0]
    band = 2 * rows
    width = (HQ // KV) * DH
    wide = pl.BlockSpec((rows, width), lambda g: (0, g))
    narrow = pl.BlockSpec((band, DH), lambda g: (0, g))
    half = pl.BlockSpec((rows, DH), lambda g: (0, g))
    half_v = pl.BlockSpec((rows, DH), lambda g: (0, g + KV))
    return pl.pallas_call(
        group_kernel,
        grid=(KV,),
        in_specs=[wide, wide, half, half_v, half, half, pl.BlockSpec((band, rows), lambda g: (0, 0))],
        out_specs=[wide, narrow, narrow],
        out_shape=[
            jax.ShapeDtypeStruct((rows, HQ * DH), jnp.bfloat16),
            jax.ShapeDtypeStruct((band, KV * DH), jnp.float32),
            jax.ShapeDtypeStruct((band, KV * DH), jnp.float32),
        ],
        interpret=INTERPRET,
    )(queries, grad_out, kv_prev, kv_prev, keys, values, mask)


def paired(dq, dk_band, dv_band, mask):
    dp_count = lax.axis_size("dp")
    seq_count = lax.axis_size("seq")
    rows = dq.shape[0]

    def route(m):
        pairs = [(d, d ^ m) for d in range(dp_count)]

        def run(ops):
            dq, dk_band, dv_band = ops
            dq = lax.ppermute(dq, "dp", pairs)
            back = jnp.concatenate([dk_band[:rows], dv_band[:rows]], axis=1)
            back = lax.ppermute(back, "seq", [(i + 1, i) for i in range(seq_count - 1)])
            own = jnp.concatenate([dk_band[rows:], dv_band[rows:]], axis=1)
            dkv = lax.ppermute((own + back).astype(jnp.bfloat16), "dp", pairs)
            return dq, dkv[:, : KV * DH], dkv[:, KV * DH :]

        return run

    return lax.switch(mask - 1, [route(m) for m in range(1, dp_count)], (dq, dk_band, dv_band))


def body(queries, keys, values, grad_out, doc_lengths, swap_mask):
    seq_count = lax.axis_size("seq")
    rows = queries.shape[0]
    s = lax.axis_index("seq")
    dp = lax.axis_index("dp")

    kv_own = jnp.concatenate([keys, values], axis=1)
    kv_prev = lax.ppermute(kv_own, "seq", [(i, i + 1) for i in range(seq_count - 1)])

    lengths = lax.dynamic_slice_in_dim(doc_lengths, dp, 1, 0)[0]
    ends = jnp.cumsum(lengths)
    q_pos = s * rows + jnp.arange(rows, dtype=jnp.int32)
    k_pos = s * rows - rows + jnp.arange(2 * rows, dtype=jnp.int32)
    seg_q = jnp.sum((ends[None, :] <= q_pos[:, None]).astype(jnp.int32), axis=1)
    seg_k = jnp.sum((ends[None, :] <= k_pos[:, None]).astype(jnp.int32), axis=1)
    allowed = (
        (k_pos[None, :] <= q_pos[:, None])
        & (k_pos[None, :] >= 0)
        & (seg_k[None, :] == seg_q[:, None])
    )

    dq, dk_band, dv_band = attention_grads(queries, grad_out, kv_prev, keys, values, allowed.T.astype(jnp.int32))
    return paired(dq, dk_band, dv_band, swap_mask[0])


def solution(mesh):
    return jax.shard_map(
        body,
        mesh=mesh,
        in_specs=(
            P(("dp", "seq"), None),
            P(("dp", "seq"), None),
            P(("dp", "seq"), None),
            P(("dp", "seq"), None),
            P(),
            P(),
        ),
        out_specs=(P(("dp", "seq"), None), P(("dp", "seq"), None), P(("dp", "seq"), None)),
        check_vma=False,
    )
```
